512 devices in a mesh: dp: 64 (over y, z), tensor: 8 (over x, core).
Axes of the slice: x: 4, y: 4, z: 16, core: 2. Of those that a mesh axis runs over, the one named last changes fastest.
Arguments:
- tokens: bfloat16 [65536, 1408], P(('dp', 'tensor')), may hold values from -6 to 6
- ln1_gain: float32 [1408], replicated, may hold values from 0.1 to 1.9
- ln1_shift: float32 [1408], replicated, may hold values from -3 to 3
- w_qkv: bfloat16 [1408, 16, 264], P(None, 'tensor')
- w_out: bfloat16 [16, 88, 1408], P('tensor'), may hold values from -0.625 to 0.625
- ln2_gain: float32 [1408], replicated, may hold values from 0.1 to 1.9
- ln2_shift: float32 [1408], replicated, may hold values from -3 to 3
- w_proj: bfloat16 [5632, 3584], P('dp', 'tensor'), may hold values from -0.078125 to 0.078125
- proj_bias: float32 [3584], P('tensor'), may hold values from -3 to 3
- segments: int32 [64, 256], P('dp'), may hold values from 0 to 7, never falling along the last dimension, each value on 1 to 128 neighbouring positions
- owners: int32 [16384, 1], P('dp'), may hold values from 0 to 63; in each aligned block of 256 rows (0 to 255, 256 to 511, ...) at most 8 rows name the same one
Outputs:
- delivered: bfloat16 [32768, 3584], P('dp', 'tensor')
The draws below stay inside these ranges and needn't reach their ends.
Inputs may be any that keep to these rules, and one draw needn't show every extreme that they name: `segments`: within a pack numbers never fall, every image has 1 to 128 groups and one has exactly that many. `owners`: among the 256 merged tokens of one pack no owner gets more than 8; in some pack an owner gets exactly 8.
All inputs are finite; a program needn't handle non-finite values.
Results may differ from the reference program's by a relative error of at most 0.015.
Values may be sent and summed in bfloat16 or wider, within the bound.
No kernel may reach another device: no remote copies, remote signals or barrier semaphores. Data moves between devices by JAX's collectives and lax.ppermute only.
A program may use at most 64 MiB of HBM per device.

```python
import math
import jax
import jax.numpy as jnp
import numpy as np
from jax import lax

D = 1408
HEADS = 16
HEAD = 88
OUT = 3584
PACK = 1024
IMGS = 8
G = 256
MERGED = 5632
CAP = 8
HGROUP = 2
TOKENS = 65536
N_DP = 64
N_TENSOR = 8


def draw_w_qkv(key, part):
    first_key = jax.random.fold_in(jax.random.fold_in(key, 11), 0)
    base = jax.random.normal(first_key, (D, HEADS, 3 * HEAD), jnp.float32) * D ** (-0.5)
    return base.astype(jnp.bfloat16)


def block_scale(own_key, shape, cuts, smallest, top_value):
    factor_of, own = 1.0, jax.random.fold_in(own_key, 6)
    for axis_at, parts in cuts:
        heights = jnp.exp(jax.random.uniform(jax.random.fold_in(own, axis_at), (parts,), jnp.float32, smallest / len(cuts), top_value / len(cuts)))
        factor_of = factor_of * jnp.repeat(heights, shape[axis_at] // parts).reshape([-1 if axis == axis_at else 1 for axis in range(len(shape))])
    return factor_of


def split_up(amount, total, limit, lean):
    weights = [(1 << 20) // math.isqrt(rank ** lean) + 1 for rank in range(2, amount + 1)]
    surplus, given = total - limit - (amount - 1), [1] * (amount - 1)
    while surplus > 0:
        candidates = [i for i in range(amount - 1) if given[i] < limit]
        mass, left = sum([weights[i] for i in candidates]), surplus
        for i in candidates:
            addition = min(limit - given[i], max(1, left * weights[i] // mass), surplus)
            given[i] = given[i] + addition
            surplus = surplus - addition
    return np.array([limit] + given)


def uneven_parts(rng, count, total, limit, lean):
    if count == 2:
        one = jax.random.randint(rng, (), max(1, total - limit), min(limit, total - 1) + 1)
        return jnp.stack([one, total - one])
    lengths = jnp.asarray(split_up(count, total, limit, lean), jnp.int32)
    pairs = (count - 1) // 2
    source_of, taker = lengths[1:1 + 2 * pairs:2], lengths[2:2 + 2 * pairs:2]
    slack = jnp.minimum(source_of - 1, limit - taker)
    shifted = jax.random.randint(jax.random.fold_in(rng, 1), (pairs,), 0, 1 << 20) % (slack + 1)
    lengths = lengths.at[1:1 + 2 * pairs:2].set(source_of - shifted).at[2:2 + 2 * pairs:2].set(taker + shifted)
    return lengths[jax.random.permutation(jax.random.fold_in(rng, 2), count)]


def assign_block(stream_key, own, number, rows, number_of, top, reach, skew):
    ranking = jax.random.permutation(stream_key, number_of)
    heavy_load, ordinary = shares(number_of, rows * top, reach, skew, True), shares(number_of, rows * top, reach, skew, False)
    places = jnp.arange(number_of)

    def named(sizes, rotation):
        used = int((sizes > 0).sum())
        fixed = max(1, used // 4)
        passed = fixed + (places - fixed + rotation * (used - fixed)) % max(1, number_of - fixed)
        return jnp.zeros((number_of,), jnp.int32).at[ranking[jnp.where(places < fixed, places, passed)]].set(jnp.asarray(sizes, jnp.int32))

    sizes = jnp.where(number % 4 == 0, named(heavy_load, number // 4), named(ordinary, number - number // 4 - 1))
    mixed = jax.random.permutation(jax.random.fold_in(own, 3), number_of)
    donor, receiver = mixed[0:number_of // 2 * 2:2], mixed[1:number_of // 2 * 2:2]
    slack = jnp.minimum(sizes[donor] - 1, reach - sizes[receiver]) // 2
    slack = jnp.where((donor == ranking[0]) | (receiver == ranking[0]) | (sizes[receiver] == 0), 0, jnp.maximum(slack, 0))
    passed = jax.random.randint(jax.random.fold_in(own, 4), (number_of // 2,), 0, 1 << 20) % (slack + 1)
    sizes = sizes.at[donor].add(-passed).at[receiver].add(passed)
    items = jnp.searchsorted(jnp.cumsum(sizes), jnp.arange(rows * top), side="right").astype(jnp.int32)
    table = items.reshape(top, rows).T
    table = table[jax.random.permutation(jax.random.fold_in(own, 1), rows)]
    rotation = jax.random.randint(jax.random.fold_in(own, 2), (rows, 1), 0, top)
    return jnp.take_along_axis(table, (jnp.arange(top)[None, :] + rotation) % top, axis=1)


def shares(number_of, total, reach, slope, full):
    portions = [(1 << 20) // math.isqrt(grade ** slope) + 1 for grade in range(1, number_of + 1)]
    largest = reach if full else min(reach, max(-(-total // number_of), total * portions[0] // sum(portions)))
    least = 1 if total - largest >= number_of - 1 else 0
    counts, spare = [largest] + [least] * (number_of - 1), total - largest - least * (number_of - 1)
    while spare > 0:
        movable = [i for i in range(1, number_of) if counts[i] < largest] or [i for i in range(1, number_of) if counts[i] < reach]
        pool, budget = sum([portions[i] for i in movable]), spare
        for i in movable:
            more = min(reach - counts[i], max(1, budget * portions[i] // pool), spare)
            counts[i] = counts[i] + more
            spare = spare - more
    return np.array(counts)


def gaussian(own_key, dims, scale, bound, cuts=(), kind=jnp.bfloat16):
    loudness = block_scale(own_key, dims, cuts, -0.22, 0.18) if cuts else 1.0
    entries = jax.random.normal(own_key, dims, jnp.float32) * scale * loudness
    return jnp.minimum(jnp.maximum(entries, -bound), bound).astype(kind)


def setup_inputs(seed: int = 0) -> dict:
    seeds = jax.random.split(jax.random.key(seed), 12)
    tokens = gaussian(seeds[0], (TOKENS, D), 1.0, 6.0, ((0, 512),))
    ln1_gain = jnp.clip(1.0 + 0.18 * jax.random.normal(seeds[1], (D,), jnp.float32), 0.1, 1.9)
    ln1_shift = gaussian(seeds[2], (D,), 0.3, 3.0, (), jnp.float32)
    w_qkv = draw_w_qkv(jax.random.fold_in(seeds[11], 71), 0)
    w_out = gaussian(seeds[4], (HEADS, HEAD, D), HEAD ** -0.5, 0.625, ((0, 8),))
    ln2_gain = jnp.clip(1.0 + 0.18 * jax.random.normal(seeds[5], (D,), jnp.float32), 0.1, 1.9)
    ln2_shift = gaussian(seeds[6], (D,), 0.3, 3.0, (), jnp.float32)
    w_proj = gaussian(seeds[7], (MERGED, OUT), MERGED ** -0.5, 0.078125, ((0, 64), (1, 8)))
    proj_bias = gaussian(seeds[8], (OUT,), 0.5, 3.0, ((0, 8),), jnp.float32)
    segments = jax.vmap(lambda own: jnp.searchsorted(jnp.cumsum(uneven_parts(own, IMGS, G, G // 2, 1)), jnp.arange(G), side="right"))(jax.random.split(seeds[9], N_DP)).reshape((N_DP, G)).astype(jnp.int32)
    owners_keys = jax.random.split(jax.random.fold_in(seeds[10], 1), (TOKENS // 4) // G)
    owners_turns = jax.random.permutation(jax.random.fold_in(seeds[10], 3), (TOKENS // 4) // G)
    owners = jax.vmap(lambda own, number: assign_block(jax.random.fold_in(seeds[10], 2), own, number, G, N_DP, 1, CAP, 2))(owners_keys, owners_turns).reshape((TOKENS // 4, 1))
    return dict(tokens=tokens, ln1_gain=ln1_gain, ln1_shift=ln1_shift, w_qkv=w_qkv, w_out=w_out, ln2_gain=ln2_gain, ln2_shift=ln2_shift, w_proj=w_proj, proj_bias=proj_bias, segments=segments, owners=owners)


def layer_norm(values, gain, shift):
    wide = values.astype(jnp.float32)
    average = lax.optimization_barrier(jnp.mean(wide, axis=-1, keepdims=True))
    centred = wide - average
    variance = lax.optimization_barrier(jnp.mean(centred * centred, axis=-1, keepdims=True))
    return centred * lax.rsqrt(variance + 1e-06) * gain + shift

def attend(heads_qkv, token_segs):
    row_count = heads_qkv.shape[0]
    width = heads_qkv.shape[2] // 3
    queries = heads_qkv[:, :, :width].astype(jnp.float32)
    keys_all = heads_qkv[:, :, width:2 * width].astype(jnp.float32)
    values_all = heads_qkv[:, :, 2 * width:].astype(jnp.float32)
    score_scale = 1.0 / jnp.sqrt(jnp.float32(width))
    block_rows = min(512, row_count)
    outputs = []
    for block_index in range(row_count // block_rows):
        lower = block_index * block_rows
        scores = jnp.einsum('qhd,khd->hqk', queries[lower:lower + block_rows], keys_all) * score_scale
        same = token_segs[lower:lower + block_rows][:, None] == token_segs[None, :]
        scores = jnp.where(same[None], scores, -jnp.inf)
        row_max = lax.optimization_barrier(jnp.max(scores, axis=-1, keepdims=True))
        exponent = jnp.exp(scores - row_max)
        probs = (exponent / lax.optimization_barrier(jnp.sum(exponent, axis=-1, keepdims=True))).astype(jnp.bfloat16)
        context = jnp.einsum('hqk,khd->qhd', probs.astype(jnp.float32), values_all)
        outputs.append(context.astype(jnp.bfloat16))
    return jnp.concatenate(outputs, axis=0)

def reference(tokens, ln1_gain, ln1_shift, w_qkv, w_out, ln2_gain, ln2_shift, w_proj, proj_bias, segments, owners):
    pack_tokens = tokens.reshape(N_DP, PACK, D)
    pack_owners = owners.reshape(N_DP, G)

    def one_pack(inputs):
        rows, segs, dests = inputs
        normed = layer_norm(rows, ln1_gain, ln1_shift).astype(jnp.bfloat16)
        heads_qkv = jnp.dot(normed, w_qkv.reshape(D, HEADS * 3 * HEAD), preferred_element_type=jnp.float32)
        heads_qkv = heads_qkv.astype(jnp.bfloat16).reshape(PACK, HEADS, 3 * HEAD)
        token_segs = jnp.repeat(segs, 4)
        context = attend(heads_qkv, token_segs)
        attn = jnp.zeros((PACK, D), jnp.float32)
        for group_index in range(N_TENSOR):
            lower = group_index * HGROUP
            term = jnp.dot(context[:, lower:lower + HGROUP].reshape(PACK, HGROUP * HEAD), w_out[lower:lower + HGROUP].reshape(HGROUP * HEAD, D), preferred_element_type=jnp.float32).astype(jnp.bfloat16)
            term = lax.optimization_barrier(term)
            attn = attn + term.astype(jnp.float32)
        hidden = (rows.astype(jnp.float32) + attn).astype(jnp.bfloat16)
        normed_two = layer_norm(hidden, ln2_gain, ln2_shift).astype(jnp.bfloat16)
        merged = normed_two.reshape(G, MERGED)
        projected = (jnp.dot(merged, w_proj, preferred_element_type=jnp.float32) + proj_bias).astype(jnp.bfloat16)
        onehot = (dests[:, None] == jnp.arange(N_DP, dtype=jnp.int32)[None, :]).astype(jnp.int32)
        earlier = jnp.cumsum(onehot, axis=0) - onehot
        position = lax.optimization_barrier(jnp.sum(earlier * onehot, axis=1)).astype(jnp.int32)
        return (projected, position)
    projected_all, positions = lax.map(one_pack, (pack_tokens, segments, pack_owners))
    pack_index = jnp.broadcast_to(jnp.arange(N_DP, dtype=jnp.int32)[:, None], (N_DP, G))
    delivered = jnp.zeros((N_DP, N_DP, CAP, OUT), jnp.bfloat16)
    delivered = delivered.at[pack_owners, pack_index, positions].set(projected_all)
    return delivered.reshape(N_DP * N_DP * CAP, OUT)
```

```python
import jax
import jax.numpy as jnp
from jax import lax
from jax.sharding import PartitionSpec as P


def layer_norm(values, gain, shift):
    wide = values.astype(jnp.float32)
    average = jnp.mean(wide, axis=-1, keepdims=True)
    centred = wide - average
    variance = jnp.mean(centred * centred, axis=-1, keepdims=True)
    return centred * lax.rsqrt(variance + 1e-06) * gain + shift


def attend(heads_qkv, token_segs):
    row_count = heads_qkv.shape[0]
    width = heads_qkv.shape[2] // 3
    queries = heads_qkv[:, :, :width]
    keys_all = heads_qkv[:, :, width : 2 * width]
    values_all = heads_qkv[:, :, 2 * width :]
    score_scale = 1.0 / jnp.sqrt(jnp.float32(width))
    block_rows = min(512, row_count)
    outputs = []
    for block_index in range(row_count // block_rows):
        lower = block_index * block_rows
        scores = (
            jnp.einsum(
                "qhd,khd->hqk",
                queries[lower : lower + block_rows],
                keys_all,
                preferred_element_type=jnp.float32,
            )
            * score_scale
        )
        same = token_segs[lower : lower + block_rows][:, None] == token_segs[None, :]
        scores = jnp.where(same[None], scores, -jnp.inf)
        row_max = jnp.max(scores, axis=-1, keepdims=True)
        exponent = jnp.exp(scores - row_max)
        probs = (exponent / jnp.sum(exponent, axis=-1, keepdims=True)).astype(jnp.bfloat16)
        context = jnp.einsum("hqk,khd->qhd", probs, values_all, preferred_element_type=jnp.float32)
        outputs.append(context.astype(jnp.bfloat16))
    return jnp.concatenate(outputs, axis=0)


def shards(
    tokens,
    ln1_gain,
    ln1_shift,
    w_qkv,
    w_out,
    ln2_gain,
    ln2_shift,
    w_proj,
    proj_bias,
    segments,
    owners,
):
    dp_count = lax.axis_size("dp")
    tp_count = lax.axis_size("tensor")
    w_proj_all = lax.all_gather(w_proj, "dp", axis=0, tiled=True)
    w_out_all = lax.all_gather(w_out, "tensor", axis=0, tiled=True)

    gathered = lax.all_gather(tokens, "tensor", axis=0, tiled=True)
    row_count = gathered.shape[0]
    local_rows = tokens.shape[0]
    normed = layer_norm(gathered, ln1_gain, ln1_shift).astype(jnp.bfloat16)
    heads_here = w_qkv.shape[1]
    heads_qkv = jnp.dot(
        normed, w_qkv.reshape(w_qkv.shape[0], -1), preferred_element_type=jnp.float32
    )
    heads_qkv = heads_qkv.astype(jnp.bfloat16).reshape(row_count, heads_here, -1)
    token_segs = jnp.repeat(segments[0], 4)
    context = attend(heads_qkv, token_segs).reshape(tp_count, local_rows, -1)
    context_mine = lax.all_to_all(context, "tensor", split_axis=0, concat_axis=0, tiled=True)
    out_heads = w_out_all.reshape(tp_count, -1, w_out_all.shape[2])
    attn = jnp.einsum(
        "sqd,sdo->qo", context_mine, out_heads, preferred_element_type=jnp.float32
    )
    hidden = (tokens.astype(jnp.float32) + attn).astype(jnp.bfloat16)
    normed_two = layer_norm(hidden, ln2_gain, ln2_shift).astype(jnp.bfloat16)
    merged_mine = normed_two.reshape(local_rows // 4, -1)
    merged = lax.all_gather(merged_mine, "tensor", axis=0, tiled=True)
    groups = merged.shape[0]
    summed = jnp.dot(merged, w_proj_all, preferred_element_type=jnp.float32)
    projected = (summed + proj_bias).astype(jnp.bfloat16)
    dests = owners[:, 0]
    onehot = (dests[:, None] == jnp.arange(dp_count, dtype=jnp.int32)[None, :]).astype(jnp.int32)
    earlier = jnp.cumsum(onehot, axis=0) - onehot
    position = jnp.sum(earlier * onehot, axis=1)
    capacity = 2 * groups // dp_count
    slot_index = dests * capacity + position
    scatter_table = (
        slot_index[None, :] == jnp.arange(dp_count * capacity, dtype=jnp.int32)[:, None]
    ).astype(jnp.bfloat16)
    outgoing = jnp.dot(scatter_table, projected, preferred_element_type=jnp.float32).astype(
        jnp.bfloat16
    )
    outgoing = outgoing.reshape(dp_count, capacity, -1)
    arrived = lax.all_to_all(outgoing, "dp", split_axis=0, concat_axis=0, tiled=True)
    return arrived.reshape(dp_count * capacity, -1)


def solution(mesh):
    return jax.shard_map(
        shards,
        mesh=mesh,
        in_specs=(
            P(("dp", "tensor"), None),
            P(),
            P(),
            P(None, "tensor", None),
            P("tensor", None, None),
            P(),
            P(),
            P("dp", "tensor"),
            P("tensor"),
            P("dp", None),
            P("dp", None),
        ),
        out_specs=P("dp", "tensor"),
        check_vma=False,
    )
```

```python
import jax
import jax.numpy as jnp
from jax import lax
from jax.sharding import Mesh, PartitionSpec as P

DP = ("y", "z")
TP = ("x", "core")


def layer_norm(values, gain, shift):
    wide = values.astype(jnp.float32)
    average = jnp.mean(wide, axis=-1, keepdims=True)
    centred = wide - average
    variance = jnp.mean(centred * centred, axis=-1, keepdims=True)
    return centred * lax.rsqrt(variance + 1e-06) * gain + shift


def attend(heads_qkv, token_segs):
    row_count = heads_qkv.shape[0]
    width = heads_qkv.shape[2] // 3
    queries = heads_qkv[:, :, :width]
    keys_all = heads_qkv[:, :, width : 2 * width]
    values_all = heads_qkv[:, :, 2 * width :]
    score_scale = 1.0 / jnp.sqrt(jnp.float32(width))
    block_rows = min(512, row_count)
    outputs = []
    for block_index in range(row_count // block_rows):
        lower = block_index * block_rows
        scores = (
            jnp.einsum(
                "qhd,khd->hqk",
                queries[lower : lower + block_rows],
                keys_all,
                preferred_element_type=jnp.float32,
            )
            * score_scale
        )
        same = token_segs[lower : lower + block_rows][:, None] == token_segs[None, :]
        scores = jnp.where(same[None], scores, -jnp.inf)
        row_max = jnp.max(scores, axis=-1, keepdims=True)
        exponent = jnp.exp(scores - row_max)
        probs = (exponent / jnp.sum(exponent, axis=-1, keepdims=True)).astype(jnp.bfloat16)
        context = jnp.einsum("hqk,khd->qhd", probs, values_all, preferred_element_type=jnp.float32)
        outputs.append(context.astype(jnp.bfloat16))
    return jnp.concatenate(outputs, axis=0)


def shards(
    tokens,
    ln1_gain,
    ln1_shift,
    w_qkv,
    w_out,
    ln2_gain,
    ln2_shift,
    w_proj,
    proj_bias,
    segments,
    owners,
):
    dp_count = (lax.axis_size("y") * lax.axis_size("z"))
    ny, nz = lax.axis_size("y"), lax.axis_size("z")
    w_zy = lax.all_gather(lax.all_gather(w_proj, "y", axis=0, tiled=True), "z", axis=0, tiled=True)
    w_proj_all = w_zy.reshape(nz, ny, -1, w_zy.shape[1]).transpose(1, 0, 2, 3).reshape(w_zy.shape)
    gathered = lax.all_gather(tokens, TP, axis=0, tiled=True)
    row_count = gathered.shape[0]
    normed = layer_norm(gathered, ln1_gain, ln1_shift).astype(jnp.bfloat16)
    heads_here = w_qkv.shape[1]
    heads_qkv = jnp.dot(
        normed, w_qkv.reshape(w_qkv.shape[0], -1), preferred_element_type=jnp.float32
    )
    heads_qkv = heads_qkv.astype(jnp.bfloat16).reshape(row_count, heads_here, -1)
    token_segs = jnp.repeat(segments[0], 4)
    context = attend(heads_qkv, token_segs).reshape(row_count, -1)
    out_flat = w_out.reshape(-1, w_out.shape[2])
    attn_all = lax.psum(
        jnp.dot(context, out_flat, preferred_element_type=jnp.float32).astype(jnp.bfloat16),
        TP,
    ).astype(jnp.float32)
    hidden = (gathered.astype(jnp.float32) + attn_all).astype(jnp.bfloat16)
    normed_all = layer_norm(hidden, ln2_gain, ln2_shift).astype(jnp.bfloat16)
    groups = row_count // 4
    merged = normed_all.reshape(groups, -1)
    summed = jnp.dot(
        merged, w_proj_all, preferred_element_type=jnp.float32
    )
    projected = (summed + proj_bias).astype(jnp.bfloat16)
    dests = owners[:, 0]
    onehot = (dests[:, None] == jnp.arange(dp_count, dtype=jnp.int32)[None, :]).astype(jnp.int32)
    earlier = jnp.cumsum(onehot, axis=0) - onehot
    position = jnp.sum(earlier * onehot, axis=1)
    capacity = 2 * groups // dp_count
    slot_index = dests * capacity + position
    scatter_table = (
        slot_index[None, :] == jnp.arange(dp_count * capacity, dtype=jnp.int32)[:, None]
    ).astype(jnp.bfloat16)
    outgoing = jnp.dot(scatter_table, projected, preferred_element_type=jnp.float32).astype(
        jnp.bfloat16
    )
    outgoing = outgoing.reshape(dp_count, capacity, -1)
    arrived = lax.all_to_all(outgoing, DP, split_axis=0, concat_axis=0, tiled=True)
    return arrived.reshape(dp_count * capacity, -1)


def solution(mesh):
    return jax.shard_map(
        shards,
        mesh=Mesh(mesh.devices.reshape(4, 16, 4, 2), ("y", "z", "x", "core")),
        in_specs=(
            P(DP + TP, None),
            P(),
            P(),
            P(None, TP, None),
            P(TP, None, None),
            P(),
            P(),
            P(DP, TP),
            P(TP),
            P(DP, None),
            P(DP, None),
        ),
        out_specs=P(DP, TP),
        check_vma=False,
    )
```

```python
import jax
import jax.numpy as jnp
from jax import lax
from jax.sharding import Mesh, PartitionSpec as P

DP = ("y", "z")
TP = ("x", "core")


def layer_norm(values, gain, shift):
    wide = values.astype(jnp.float32)
    average = jnp.mean(wide, axis=-1, keepdims=True)
    centred = wide - average
    variance = jnp.mean(centred * centred, axis=-1, keepdims=True)
    return centred * lax.rsqrt(variance + 1e-06) * gain + shift


def attend(heads_qkv, token_segs):
    row_count = heads_qkv.shape[0]
    width = heads_qkv.shape[2] // 3
    queries = heads_qkv[:, :, :width]
    keys_all = heads_qkv[:, :, width : 2 * width]
    values_all = heads_qkv[:, :, 2 * width :]
    score_scale = 1.0 / jnp.sqrt(jnp.float32(width))
    block_rows = min(512, row_count)
    outputs = []
    for block_index in range(row_count // block_rows):
        lower = block_index * block_rows
        scores = (
            jnp.einsum(
                "qhd,khd->hqk",
                queries[lower : lower + block_rows],
                keys_all,
                preferred_element_type=jnp.float32,
            )
            * score_scale
        )
        same = token_segs[lower : lower + block_rows][:, None] == token_segs[None, :]
        scores = jnp.where(same[None], scores, -jnp.inf)
        row_max = jnp.max(scores, axis=-1, keepdims=True)
        exponent = jnp.exp(scores - row_max)
        probs = (exponent / jnp.sum(exponent, axis=-1, keepdims=True)).astype(jnp.bfloat16)
        context = jnp.einsum("hqk,khd->qhd", probs, values_all, preferred_element_type=jnp.float32)
        outputs.append(context.astype(jnp.bfloat16))
    return jnp.concatenate(outputs, axis=0)


def shards(
    tokens,
    ln1_gain,
    ln1_shift,
    w_qkv,
    w_out,
    ln2_gain,
    ln2_shift,
    w_proj,
    proj_bias,
    segments,
    owners,
):
    dp_count = (lax.axis_size("y") * lax.axis_size("z"))
    ny, nz = lax.axis_size("y"), lax.axis_size("z")
    w_y = lax.all_gather(w_proj, "y", axis=0)
    w_proj_all = lax.all_gather(w_y, "z", axis=1).reshape(-1, w_proj.shape[1])
    gathered = lax.all_gather(tokens, TP, axis=0, tiled=True)
    row_count = gathered.shape[0]
    normed = layer_norm(gathered, ln1_gain, ln1_shift).astype(jnp.bfloat16)
    heads_here = w_qkv.shape[1]
    heads_qkv = jnp.dot(
        normed, w_qkv.reshape(w_qkv.shape[0], -1), preferred_element_type=jnp.float32
    )
    heads_qkv = heads_qkv.astype(jnp.bfloat16).reshape(row_count, heads_here, -1)
    token_segs = jnp.repeat(segments[0], 4)
    context = attend(heads_qkv, token_segs).reshape(row_count, -1)
    out_flat = w_out.reshape(-1, w_out.shape[2])
    attn_all = lax.psum(
        jnp.dot(context, out_flat, preferred_element_type=jnp.float32).astype(jnp.bfloat16),
        TP,
    ).astype(jnp.float32)
    hidden = (gathered.astype(jnp.float32) + attn_all).astype(jnp.bfloat16)
    normed_all = layer_norm(hidden, ln2_gain, ln2_shift).astype(jnp.bfloat16)
    groups = row_count // 4
    merged = normed_all.reshape(groups, -1)
    summed = jnp.dot(
        merged, w_proj_all, preferred_element_type=jnp.float32
    )
    projected = (summed + proj_bias).astype(jnp.bfloat16)
    dests = owners[:, 0]
    onehot = (dests[:, None] == jnp.arange(dp_count, dtype=jnp.int32)[None, :]).astype(jnp.int32)
    earlier = jnp.cumsum(onehot, axis=0) - onehot
    position = jnp.sum(earlier * onehot, axis=1)
    capacity = 2 * groups // dp_count
    slot_index = dests * capacity + position
    scatter_table = (
        slot_index[None, :] == jnp.arange(dp_count * capacity, dtype=jnp.int32)[:, None]
    ).astype(jnp.bfloat16)
    outgoing = jnp.dot(scatter_table, projected, preferred_element_type=jnp.float32).astype(
        jnp.bfloat16
    )
    outgoing = outgoing.reshape(dp_count, capacity, -1)
    arrived = lax.all_to_all(outgoing, DP, split_axis=0, concat_axis=0, tiled=True)
    return arrived.reshape(dp_count * capacity, -1)


def solution(mesh):
    return jax.shard_map(
        shards,
        mesh=Mesh(mesh.devices.reshape(4, 16, 4, 2), ("y", "z", "x", "core")),
        in_specs=(
            P(DP + TP, None),
            P(),
            P(),
            P(None, TP, None),
            P(TP, None, None),
            P(),
            P(),
            P(DP, TP),
            P(TP),
            P(DP, None),
            P(DP, None),
        ),
        out_specs=P(DP, TP),
        check_vma=False,
    )
```

```python
import jax
import jax.numpy as jnp
from jax import lax
from jax.sharding import Mesh, PartitionSpec as P

DP = ("y", "z")
TP = ("x", "core")


def layer_norm(values, gain, shift):
    wide = values.astype(jnp.float32)
    average = jnp.mean(wide, axis=-1, keepdims=True)
    centred = wide - average
    variance = jnp.mean(centred * centred, axis=-1, keepdims=True)
    return centred * lax.rsqrt(variance + 1e-06) * gain + shift


def attend(heads_qkv, token_segs):
    row_count = heads_qkv.shape[0]
    width = heads_qkv.shape[2] // 3
    queries = heads_qkv[:, :, :width]
    keys_all = heads_qkv[:, :, width : 2 * width]
    values_all = heads_qkv[:, :, 2 * width :]
    score_scale = 1.0 / jnp.sqrt(jnp.float32(width))
    block_rows = min(512, row_count)
    outputs = []
    for block_index in range(row_count // block_rows):
        lower = block_index * block_rows
        scores = (
            jnp.einsum(
                "qhd,khd->hqk",
                queries[lower : lower + block_rows],
                keys_all,
                preferred_element_type=jnp.float32,
            )
            * score_scale
        )
        same = token_segs[lower : lower + block_rows][:, None] == token_segs[None, :]
        scores = jnp.where(same[None], scores, -jnp.inf)
        row_max = jnp.max(scores, axis=-1, keepdims=True)
        exponent = jnp.exp(scores - row_max)
        probs = (exponent / jnp.sum(exponent, axis=-1, keepdims=True)).astype(jnp.bfloat16)
        context = jnp.einsum("hqk,khd->qhd", probs, values_all, preferred_element_type=jnp.float32)
        outputs.append(context.astype(jnp.bfloat16))
    return jnp.concatenate(outputs, axis=0)


def shards(
    tokens,
    ln1_gain,
    ln1_shift,
    w_qkv,
    w_out,
    ln2_gain,
    ln2_shift,
    w_proj,
    proj_bias,
    segments,
    owners,
):
    dp_count = (lax.axis_size("y") * lax.axis_size("z"))
    ny, nz = lax.axis_size("y"), lax.axis_size("z")
    w_y = lax.all_gather(w_proj, "y", axis=0)
    w_proj_all = lax.all_gather(w_y, "z", axis=1).reshape(-1, w_proj.shape[1])
    gathered = lax.all_gather(tokens, TP, axis=0, tiled=True)
    row_count = gathered.shape[0]
    normed = layer_norm(gathered, ln1_gain, ln1_shift).astype(jnp.bfloat16)
    heads_here = w_qkv.shape[1]
    heads_qkv = jnp.dot(
        normed, w_qkv.reshape(w_qkv.shape[0], -1), preferred_element_type=jnp.float32
    )
    heads_qkv = heads_qkv.astype(jnp.bfloat16).reshape(row_count, heads_here, -1)
    token_segs = jnp.repeat(segments[0], 4)
    context = attend(heads_qkv, token_segs).reshape(row_count, -1)
    out_flat = w_out.reshape(-1, w_out.shape[2])
    term = jnp.dot(context, out_flat, preferred_element_type=jnp.float32).astype(jnp.bfloat16)
    tp_count = lax.axis_size("x") * lax.axis_size("core")
    local_rows = tokens.shape[0]
    terms_mine = lax.all_to_all(term.reshape(tp_count, local_rows, -1), TP, 0, 0, tiled=True)
    attn = jnp.sum(terms_mine.astype(jnp.float32), axis=0)
    hidden = (tokens.astype(jnp.float32) + attn).astype(jnp.bfloat16)
    normed_two = layer_norm(hidden, ln2_gain, ln2_shift).astype(jnp.bfloat16)
    merged_mine = normed_two.reshape(local_rows // 4, -1)
    copies = jnp.broadcast_to(merged_mine[None], (tp_count,) + merged_mine.shape)
    merged = lax.all_to_all(copies, TP, 0, 0, tiled=True).reshape(-1, merged_mine.shape[1])
    groups = merged.shape[0]
    summed = jnp.dot(
        merged, w_proj_all, preferred_element_type=jnp.float32
    )
    projected = (summed + proj_bias).astype(jnp.bfloat16)
    dests = owners[:, 0]
    onehot = (dests[:, None] == jnp.arange(dp_count, dtype=jnp.int32)[None, :]).astype(jnp.int32)
    earlier = jnp.cumsum(onehot, axis=0) - onehot
    position = jnp.sum(earlier * onehot, axis=1)
    capacity = 2 * groups // dp_count
    slot_index = dests * capacity + position
    scatter_table = (
        slot_index[None, :] == jnp.arange(dp_count * capacity, dtype=jnp.int32)[:, None]
    ).astype(jnp.bfloat16)
    outgoing = jnp.dot(scatter_table, projected, preferred_element_type=jnp.float32).astype(
        jnp.bfloat16
    )
    outgoing = outgoing.reshape(dp_count, capacity, -1)
    arrived = lax.all_to_all(outgoing, DP, split_axis=0, concat_axis=0, tiled=True)
    return arrived.reshape(dp_count * capacity, -1)


def solution(mesh):
    return jax.shard_map(
        shards,
        mesh=Mesh(mesh.devices.reshape(4, 16, 4, 2), ("y", "z", "x", "core")),
        in_specs=(
            P(DP + TP, None),
            P(),
            P(),
            P(None, TP, None),
            P(TP, None, None),
            P(),
            P(),
            P(DP, TP),
            P(TP),
            P(DP, None),
            P(DP, None),
        ),
        out_specs=P(DP, TP),
        check_vma=False,
    )
```

```python
import jax
import jax.numpy as jnp
from jax import lax
from jax.sharding import Mesh, PartitionSpec as P

DP = ("y", "z")
TP = ("x", "core")


def layer_norm(values, gain, shift):
    wide = values.astype(jnp.float32)
    average = jnp.mean(wide, axis=-1, keepdims=True)
    centred = wide - average
    variance = jnp.mean(centred * centred, axis=-1, keepdims=True)
    return centred * lax.rsqrt(variance + 1e-06) * gain + shift


def attend(heads_qkv, token_segs):
    row_count = heads_qkv.shape[0]
    width = heads_qkv.shape[2] // 3
    queries = heads_qkv[:, :, :width]
    keys_all = heads_qkv[:, :, width : 2 * width]
    values_all = heads_qkv[:, :, 2 * width :]
    score_scale = 1.0 / jnp.sqrt(jnp.float32(width))
    block_rows = min(512, row_count)
    outputs = []
    for block_index in range(row_count // block_rows):
        lower = block_index * block_rows
        scores = (
            jnp.einsum(
                "qhd,khd->hqk",
                queries[lower : lower + block_rows],
                keys_all,
                preferred_element_type=jnp.float32,
            )
            * score_scale
        )
        same = token_segs[lower : lower + block_rows][:, None] == token_segs[None, :]
        scores = jnp.where(same[None], scores, -jnp.inf)
        row_max = jnp.max(scores, axis=-1, keepdims=True)
        exponent = jnp.exp(scores - row_max)
        probs = (exponent / jnp.sum(exponent, axis=-1, keepdims=True)).astype(jnp.bfloat16)
        context = jnp.einsum("hqk,khd->qhd", probs, values_all, preferred_element_type=jnp.float32)
        outputs.append(context.astype(jnp.bfloat16))
    return jnp.concatenate(outputs, axis=0)


def shards(
    tokens,
    ln1_gain,
    ln1_shift,
    w_qkv,
    w_out,
    ln2_gain,
    ln2_shift,
    w_proj,
    proj_bias,
    segments,
    owners,
):
    dp_count = (lax.axis_size("y") * lax.axis_size("z"))
    ny, nz = lax.axis_size("y"), lax.axis_size("z")
    w_y = lax.all_gather(w_proj, "y", axis=0)
    w_proj_all = lax.all_gather(w_y, "z", axis=1).reshape(-1, w_proj.shape[1])
    normed_mine = layer_norm(tokens, ln1_gain, ln1_shift).astype(jnp.bfloat16)
    normed = lax.all_gather(normed_mine, TP, axis=0, tiled=True)
    row_count = normed.shape[0]
    heads_here = w_qkv.shape[1]
    heads_qkv = jnp.dot(
        normed, w_qkv.reshape(w_qkv.shape[0], -1), preferred_element_type=jnp.float32
    )
    heads_qkv = heads_qkv.astype(jnp.bfloat16).reshape(row_count, heads_here, -1)
    token_segs = jnp.repeat(segments[0], 4)
    context = attend(heads_qkv, token_segs).reshape(row_count, -1)
    out_flat = w_out.reshape(-1, w_out.shape[2])
    term = jnp.dot(context, out_flat, preferred_element_type=jnp.float32).astype(jnp.bfloat16)
    tp_count = lax.axis_size("x") * lax.axis_size("core")
    local_rows = tokens.shape[0]
    terms_mine = lax.all_to_all(term.reshape(tp_count, local_rows, -1), TP, 0, 0, tiled=True)
    attn = jnp.sum(terms_mine.astype(jnp.float32), axis=0)
    hidden = (tokens.astype(jnp.float32) + attn).astype(jnp.bfloat16)
    normed_two = layer_norm(hidden, ln2_gain, ln2_shift).astype(jnp.bfloat16)
    merged_mine = normed_two.reshape(local_rows // 4, -1)
    copies = jnp.broadcast_to(merged_mine[None], (tp_count,) + merged_mine.shape)
    merged = lax.all_to_all(copies, TP, 0, 0, tiled=True).reshape(-1, merged_mine.shape[1])
    groups = merged.shape[0]
    summed = jnp.dot(
        merged, w_proj_all, preferred_element_type=jnp.float32
    )
    projected = (summed + proj_bias).astype(jnp.bfloat16)
    dests = owners[:, 0]
    onehot = (dests[:, None] == jnp.arange(dp_count, dtype=jnp.int32)[None, :]).astype(jnp.int32)
    earlier = jnp.cumsum(onehot, axis=0) - onehot
    position = jnp.sum(earlier * onehot, axis=1)
    capacity = 2 * groups // dp_count
    slot_index = dests * capacity + position
    scatter_table = (
        slot_index[None, :] == jnp.arange(dp_count * capacity, dtype=jnp.int32)[:, None]
    ).astype(jnp.bfloat16)
    outgoing = jnp.dot(scatter_table, projected, preferred_element_type=jnp.float32).astype(
        jnp.bfloat16
    )
    outgoing = outgoing.reshape(dp_count, capacity, -1)
    arrived = lax.all_to_all(outgoing, DP, split_axis=0, concat_axis=0, tiled=True)
    return arrived.reshape(dp_count * capacity, -1)


def solution(mesh):
    return jax.shard_map(
        shards,
        mesh=Mesh(mesh.devices.reshape(4, 16, 4, 2), ("y", "z", "x", "core")),
        in_specs=(
            P(DP + TP, None),
            P(),
            P(),
            P(None, TP, None),
            P(TP, None, None),
            P(),
            P(),
            P(DP, TP),
            P(TP),
            P(DP, None),
            P(DP, None),
        ),
        out_specs=P(DP, TP),
        check_vma=False,
    )
```

```python
import jax
import jax.numpy as jnp
from jax import lax
from jax.sharding import Mesh, PartitionSpec as P

DP = ("y", "z")
TP = ("x", "core")


def layer_norm(values, gain, shift):
    wide = values.astype(jnp.float32)
    average = jnp.mean(wide, axis=-1, keepdims=True)
    centred = wide - average
    variance = jnp.mean(centred * centred, axis=-1, keepdims=True)
    return centred * lax.rsqrt(variance + 1e-06) * gain + shift


def attend(heads_qkv, token_segs):
    row_count = heads_qkv.shape[0]
    width = heads_qkv.shape[2] // 3
    queries = heads_qkv[:, :, :width]
    keys_all = heads_qkv[:, :, width : 2 * width]
    values_all = heads_qkv[:, :, 2 * width :]
    score_scale = 1.0 / jnp.sqrt(jnp.float32(width))
    block_rows = min(512, row_count)
    outputs = []
    for block_index in range(row_count // block_rows):
        lower = block_index * block_rows
        scores = (
            jnp.einsum(
                "qhd,khd->hqk",
                queries[lower : lower + block_rows],
                keys_all,
                preferred_element_type=jnp.float32,
            )
            * score_scale
        )
        same = token_segs[lower : lower + block_rows][:, None] == token_segs[None, :]
        scores = jnp.where(same[None], scores, -jnp.inf)
        row_max = jnp.max(scores, axis=-1, keepdims=True)
        exponent = jnp.exp(scores - row_max)
        probs = (exponent / jnp.sum(exponent, axis=-1, keepdims=True)).astype(jnp.bfloat16)
        context = jnp.einsum("hqk,khd->qhd", probs, values_all, preferred_element_type=jnp.float32)
        outputs.append(context.astype(jnp.bfloat16))
    return jnp.concatenate(outputs, axis=0)


def shards(
    tokens,
    ln1_gain,
    ln1_shift,
    w_qkv,
    w_out,
    ln2_gain,
    ln2_shift,
    w_proj,
    proj_bias,
    segments,
    owners,
):
    dp_count = (lax.axis_size("y") * lax.axis_size("z"))
    ny, nz = lax.axis_size("y"), lax.axis_size("z")
    w_y = lax.all_gather(w_proj, "y", axis=0)
    w_proj_all = lax.all_gather(w_y, "z", axis=1).reshape(-1, w_proj.shape[1])
    gathered = lax.all_gather(tokens, TP, axis=0, tiled=True)
    tp_n = lax.axis_size("x") * lax.axis_size("core")
    w_out_all = lax.all_to_all(jnp.broadcast_to(w_out[None], (tp_n,) + w_out.shape), TP, 0, 0, tiled=True)
    w_out_all = w_out_all.reshape((-1,) + w_out.shape[1:])
    row_count = gathered.shape[0]
    normed = layer_norm(gathered, ln1_gain, ln1_shift).astype(jnp.bfloat16)
    heads_here = w_qkv.shape[1]
    heads_qkv = jnp.dot(
        normed, w_qkv.reshape(w_qkv.shape[0], -1), preferred_element_type=jnp.float32
    )
    heads_qkv = heads_qkv.astype(jnp.bfloat16).reshape(row_count, heads_here, -1)
    token_segs = jnp.repeat(segments[0], 4)
    context = attend(heads_qkv, token_segs).reshape(row_count, -1)
    tp_count = lax.axis_size("x") * lax.axis_size("core")
    local_rows = tokens.shape[0]
    context_mine = lax.all_to_all(context.reshape(tp_count, local_rows, -1), TP, 0, 0, tiled=True)
    out_heads = w_out_all.reshape(tp_count, -1, w_out_all.shape[2])
    attn = jnp.einsum("sqd,sdo->qo", context_mine, out_heads, preferred_element_type=jnp.float32)
    hidden = (tokens.astype(jnp.float32) + attn).astype(jnp.bfloat16)
    normed_two = layer_norm(hidden, ln2_gain, ln2_shift).astype(jnp.bfloat16)
    merged_mine = normed_two.reshape(local_rows // 4, -1)
    copies = jnp.broadcast_to(merged_mine[None], (tp_count,) + merged_mine.shape)
    merged = lax.all_to_all(copies, TP, 0, 0, tiled=True).reshape(-1, merged_mine.shape[1])
    groups = merged.shape[0]
    summed = jnp.dot(
        merged, w_proj_all, preferred_element_type=jnp.float32
    )
    projected = (summed + proj_bias).astype(jnp.bfloat16)
    dests = owners[:, 0]
    onehot = (dests[:, None] == jnp.arange(dp_count, dtype=jnp.int32)[None, :]).astype(jnp.int32)
    earlier = jnp.cumsum(onehot, axis=0) - onehot
    position = jnp.sum(earlier * onehot, axis=1)
    capacity = 2 * groups // dp_count
    slot_index = dests * capacity + position
    scatter_table = (
        slot_index[None, :] == jnp.arange(dp_count * capacity, dtype=jnp.int32)[:, None]
    ).astype(jnp.bfloat16)
    outgoing = jnp.dot(scatter_table, projected, preferred_element_type=jnp.float32).astype(
        jnp.bfloat16
    )
    outgoing = outgoing.reshape(dp_count, capacity, -1)
    arrived = lax.all_to_all(outgoing, DP, split_axis=0, concat_axis=0, tiled=True)
    return arrived.reshape(dp_count * capacity, -1)


def solution(mesh):
    return jax.shard_map(
        shards,
        mesh=Mesh(mesh.devices.reshape(4, 16, 4, 2), ("y", "z", "x", "core")),
        in_specs=(
            P(DP + TP, None),
            P(),
            P(),
            P(None, TP, None),
            P(TP, None, None),
            P(),
            P(),
            P(DP, TP),
            P(TP),
            P(DP, None),
            P(DP, None),
        ),
        out_specs=P(DP, TP),
        check_vma=False,
    )
```

```python
import jax
import jax.numpy as jnp
from jax import lax
from jax.sharding import Mesh, PartitionSpec as P

DP = ("y", "z")
TP = ("x", "core")


def layer_norm(values, gain, shift):
    wide = values.astype(jnp.float32)
    average = jnp.mean(wide, axis=-1, keepdims=True)
    centred = wide - average
    variance = jnp.mean(centred * centred, axis=-1, keepdims=True)
    return centred * lax.rsqrt(variance + 1e-06) * gain + shift


def attend(heads_qkv, token_segs):
    row_count = heads_qkv.shape[0]
    width = heads_qkv.shape[2] // 3
    queries = heads_qkv[:, :, :width]
    keys_all = heads_qkv[:, :, width : 2 * width]
    values_all = heads_qkv[:, :, 2 * width :]
    score_scale = 1.0 / jnp.sqrt(jnp.float32(width))
    block_rows = min(512, row_count)
    outputs = []
    for block_index in range(row_count // block_rows):
        lower = block_index * block_rows
        scores = (
            jnp.einsum(
                "qhd,khd->hqk",
                queries[lower : lower + block_rows],
                keys_all,
                preferred_element_type=jnp.float32,
            )
            * score_scale
        )
        same = token_segs[lower : lower + block_rows][:, None] == token_segs[None, :]
        scores = jnp.where(same[None], scores, -jnp.inf)
        row_max = jnp.max(scores, axis=-1, keepdims=True)
        exponent = jnp.exp(scores - row_max)
        probs = (exponent / jnp.sum(exponent, axis=-1, keepdims=True)).astype(jnp.bfloat16)
        context = jnp.einsum("hqk,khd->qhd", probs, values_all, preferred_element_type=jnp.float32)
        outputs.append(context.astype(jnp.bfloat16))
    return jnp.concatenate(outputs, axis=0)


def shards(
    tokens,
    ln1_gain,
    ln1_shift,
    w_qkv,
    w_out,
    ln2_gain,
    ln2_shift,
    w_proj,
    proj_bias,
    segments,
    owners,
):
    dp_count = (lax.axis_size("y") * lax.axis_size("z"))
    ny, nz = lax.axis_size("y"), lax.axis_size("z")
    w_y = lax.all_gather(w_proj, "y", axis=0)
    w_proj_all = lax.all_gather(w_y, "z", axis=1).reshape(-1, w_proj.shape[1])
    gathered = lax.all_gather(tokens, TP, axis=0, tiled=True)
    tp_n = lax.axis_size("x") * lax.axis_size("core")
    nx, nc = lax.axis_size("x"), lax.axis_size("core")
    w_out_x = lax.all_to_all(jnp.broadcast_to(w_out[None], (nx,) + w_out.shape), "x", 0, 0, tiled=True)
    w_out_all = lax.all_to_all(jnp.broadcast_to(w_out_x[None], (nc,) + w_out_x.shape), "core", 0, 0, tiled=True)
    row_count = gathered.shape[0]
    normed = layer_norm(gathered, ln1_gain, ln1_shift).astype(jnp.bfloat16)
    heads_here = w_qkv.shape[1]
    heads_qkv = jnp.dot(
        normed, w_qkv.reshape(w_qkv.shape[0], -1), preferred_element_type=jnp.float32
    )
    heads_qkv = heads_qkv.astype(jnp.bfloat16).reshape(row_count, heads_here, -1)
    token_segs = jnp.repeat(segments[0], 4)
    context = attend(heads_qkv, token_segs).reshape(row_count, -1)
    tp_count = lax.axis_size("x") * lax.axis_size("core")
    local_rows = tokens.shape[0]
    context_mine = lax.all_to_all(context.reshape(tp_count, local_rows, -1), TP, 0, 0, tiled=True)
    out_heads = w_out_all.reshape(nc, nx, -1, w_out_all.shape[-1])
    context_xc = context_mine.reshape(nx, nc, local_rows, -1)
    attn = jnp.einsum("xcqd,cxdo->qo", context_xc, out_heads, preferred_element_type=jnp.float32)
    hidden = (tokens.astype(jnp.float32) + attn).astype(jnp.bfloat16)
    normed_two = layer_norm(hidden, ln2_gain, ln2_shift).astype(jnp.bfloat16)
    merged_mine = normed_two.reshape(local_rows // 4, -1)
    copies = jnp.broadcast_to(merged_mine[None], (tp_count,) + merged_mine.shape)
    merged = lax.all_to_all(copies, TP, 0, 0, tiled=True).reshape(-1, merged_mine.shape[1])
    groups = merged.shape[0]
    summed = jnp.dot(
        merged, w_proj_all, preferred_element_type=jnp.float32
    )
    projected = (summed + proj_bias).astype(jnp.bfloat16)
    dests = owners[:, 0]
    onehot = (dests[:, None] == jnp.arange(dp_count, dtype=jnp.int32)[None, :]).astype(jnp.int32)
    earlier = jnp.cumsum(onehot, axis=0) - onehot
    position = jnp.sum(earlier * onehot, axis=1)
    capacity = 2 * groups // dp_count
    slot_index = dests * capacity + position
    scatter_table = (
        slot_index[None, :] == jnp.arange(dp_count * capacity, dtype=jnp.int32)[:, None]
    ).astype(jnp.bfloat16)
    outgoing = jnp.dot(scatter_table, projected, preferred_element_type=jnp.float32).astype(
        jnp.bfloat16
    )
    outgoing = outgoing.reshape(dp_count, capacity, -1)
    arrived = lax.all_to_all(outgoing, DP, split_axis=0, concat_axis=0, tiled=True)
    return arrived.reshape(dp_count * capacity, -1)


def solution(mesh):
    return jax.shard_map(
        shards,
        mesh=Mesh(mesh.devices.reshape(4, 16, 4, 2), ("y", "z", "x", "core")),
        in_specs=(
            P(DP + TP, None),
            P(),
            P(),
            P(None, TP, None),
            P(TP, None, None),
            P(),
            P(),
            P(DP, TP),
            P(TP),
            P(DP, None),
            P(DP, None),
        ),
        out_specs=P(DP, TP),
        check_vma=False,
    )
```

```python
import jax
import jax.numpy as jnp
from jax import lax
from jax.sharding import Mesh, PartitionSpec as P

DP = ("y", "z")
TP = ("x", "core")


def layer_norm(values, gain, shift):
    wide = values.astype(jnp.float32)
    average = jnp.mean(wide, axis=-1, keepdims=True)
    centred = wide - average
    variance = jnp.mean(centred * centred, axis=-1, keepdims=True)
    return centred * lax.rsqrt(variance + 1e-06) * gain + shift


def attend(heads_qkv, token_segs):
    row_count = heads_qkv.shape[0]
    width = heads_qkv.shape[2] // 3
    queries = heads_qkv[:, :, :width]
    keys_all = heads_qkv[:, :, width : 2 * width]
    values_all = heads_qkv[:, :, 2 * width :]
    score_scale = 1.0 / jnp.sqrt(jnp.float32(width))
    block_rows = min(512, row_count)
    outputs = []
    for block_index in range(row_count // block_rows):
        lower = block_index * block_rows
        scores = (
            jnp.einsum(
                "qhd,khd->hqk",
                queries[lower : lower + block_rows],
                keys_all,
                preferred_element_type=jnp.float32,
            )
            * score_scale
        )
        same = token_segs[lower : lower + block_rows][:, None] == token_segs[None, :]
        scores = jnp.where(same[None], scores, -jnp.inf)
        row_max = jnp.max(scores, axis=-1, keepdims=True)
        exponent = jnp.exp(scores - row_max)
        probs = (exponent / jnp.sum(exponent, axis=-1, keepdims=True)).astype(jnp.bfloat16)
        context = jnp.einsum("hqk,khd->qhd", probs, values_all, preferred_element_type=jnp.float32)
        outputs.append(context.astype(jnp.bfloat16))
    return jnp.concatenate(outputs, axis=0)


def shards(
    tokens,
    ln1_gain,
    ln1_shift,
    w_qkv,
    w_out,
    ln2_gain,
    ln2_shift,
    w_proj,
    proj_bias,
    segments,
    owners,
):
    dp_count = (lax.axis_size("y") * lax.axis_size("z"))
    ny, nz = lax.axis_size("y"), lax.axis_size("z")
    w_y = lax.all_gather(w_proj, "y", axis=0)
    w_proj_all = lax.all_gather(w_y, "z", axis=1).reshape(-1, w_proj.shape[1])
    gathered = lax.all_gather(tokens, TP, axis=0, tiled=True)
    tp_n = lax.axis_size("x") * lax.axis_size("core")
    nx, nc = lax.axis_size("x"), lax.axis_size("core")
    w_out_x = lax.all_to_all(jnp.broadcast_to(w_out[None], (nx,) + w_out.shape), "x", 0, 0, tiled=True)
    w_out_all = lax.all_to_all(jnp.broadcast_to(w_out_x[None], (nc,) + w_out_x.shape), "core", 0, 0, tiled=True)
    row_count = gathered.shape[0]
    normed = layer_norm(gathered, ln1_gain, ln1_shift).astype(jnp.bfloat16)
    heads_here = w_qkv.shape[1]
    heads_qkv = jnp.dot(
        normed, w_qkv.reshape(w_qkv.shape[0], -1), preferred_element_type=jnp.float32
    )
    heads_qkv = heads_qkv.astype(jnp.bfloat16).reshape(row_count, heads_here, -1)
    token_segs = jnp.repeat(segments[0], 4)
    context = attend(heads_qkv, token_segs).reshape(row_count, -1)
    tp_count = lax.axis_size("x") * lax.axis_size("core")
    local_rows = tokens.shape[0]
    context_mine = lax.all_to_all(context.reshape(tp_count, local_rows, -1), TP, 0, 0, tiled=True)
    out_heads = w_out_all.reshape(nc, nx, -1, w_out_all.shape[-1])
    context_xc = context_mine.reshape(nx, nc, local_rows, -1)
    attn = jnp.einsum("xcqd,cxdo->qo", context_xc, out_heads, preferred_element_type=jnp.float32)
    hidden = (tokens.astype(jnp.float32) + attn).astype(jnp.bfloat16)
    normed_two = layer_norm(hidden, ln2_gain, ln2_shift).astype(jnp.bfloat16)
    merged_mine = normed_two.reshape(local_rows // 4, -1)
    copies = jnp.broadcast_to(merged_mine[None], (nx,) + merged_mine.shape)
    merged_x = lax.all_to_all(copies, "x", 0, 0, tiled=True)
    pair = jnp.broadcast_to(merged_x[None], (nc,) + merged_x.shape)
    merged = lax.all_to_all(pair, "core", 0, 0, tiled=True).reshape(-1, merged_mine.shape[1])
    groups = merged.shape[0]
    summed = jnp.dot(
        merged, w_proj_all, preferred_element_type=jnp.float32
    )
    projected = (summed + proj_bias).astype(jnp.bfloat16)
    dests = owners[:, 0]
    onehot = (dests[:, None] == jnp.arange(dp_count, dtype=jnp.int32)[None, :]).astype(jnp.int32)
    earlier = jnp.cumsum(onehot, axis=0) - onehot
    position = jnp.sum(earlier * onehot, axis=1)
    capacity = 2 * groups // dp_count
    slot_index = dests * capacity + position
    slot_index = slot_index.reshape(nx, nc, -1).transpose(1, 0, 2).reshape(-1)
    scatter_table = (
        slot_index[None, :] == jnp.arange(dp_count * capacity, dtype=jnp.int32)[:, None]
    ).astype(jnp.bfloat16)
    outgoing = jnp.dot(scatter_table, projected, preferred_element_type=jnp.float32).astype(
        jnp.bfloat16
    )
    outgoing = outgoing.reshape(dp_count, capacity, -1)
    arrived = lax.all_to_all(outgoing, DP, split_axis=0, concat_axis=0, tiled=True)
    return arrived.reshape(dp_count * capacity, -1)


def solution(mesh):
    return jax.shard_map(
        shards,
        mesh=Mesh(mesh.devices.reshape(4, 16, 4, 2), ("y", "z", "x", "core")),
        in_specs=(
            P(DP + TP, None),
            P(),
            P(),
            P(None, TP, None),
            P(TP, None, None),
            P(),
            P(),
            P(DP, TP),
            P(TP),
            P(DP, None),
            P(DP, None),
        ),
        out_specs=P(DP, TP),
        check_vma=False,
    )
```

```python
import jax
import jax.numpy as jnp
from jax import lax
from jax.sharding import Mesh, PartitionSpec as P

DP = ("y", "z")
IMAGE_TOKENS = 512
TP = ("x", "core")


def layer_norm(values, gain, shift):
    wide = values.astype(jnp.float32)
    average = jnp.mean(wide, axis=-1, keepdims=True)
    centred = wide - average
    variance = jnp.mean(centred * centred, axis=-1, keepdims=True)
    return centred * lax.rsqrt(variance + 1e-06) * gain + shift


def attend(heads_qkv, token_segs):
    row_count = heads_qkv.shape[0]
    width = heads_qkv.shape[2] // 3
    queries = heads_qkv[:, :, :width]
    keys_all = heads_qkv[:, :, width : 2 * width]
    values_all = heads_qkv[:, :, 2 * width :]
    score_scale = 1.0 / jnp.sqrt(jnp.float32(width))
    block_rows = min(256, row_count)
    outputs = []
    for block_index in range(row_count // block_rows):
        lower = block_index * block_rows
        key_lo = max(0, lower - IMAGE_TOKENS + 1) // 128 * 128
        key_hi = min(row_count, -(-(lower + block_rows + IMAGE_TOKENS - 1) // 128) * 128)
        scores = (
            jnp.einsum(
                "qhd,khd->hqk",
                queries[lower : lower + block_rows],
                keys_all[key_lo:key_hi],
                preferred_element_type=jnp.float32,
            )
            * score_scale
        )
        same = token_segs[lower : lower + block_rows][:, None] == token_segs[None, key_lo:key_hi]
        scores = jnp.where(same[None], scores, -jnp.inf)
        row_max = jnp.max(scores, axis=-1, keepdims=True)
        exponent = jnp.exp(scores - row_max)
        probs = (exponent / jnp.sum(exponent, axis=-1, keepdims=True)).astype(jnp.bfloat16)
        context = jnp.einsum(
            "hqk,khd->qhd", probs, values_all[key_lo:key_hi], preferred_element_type=jnp.float32
        )
        outputs.append(context.astype(jnp.bfloat16))
    return jnp.concatenate(outputs, axis=0)


def shards(
    tokens,
    ln1_gain,
    ln1_shift,
    w_qkv,
    w_out,
    ln2_gain,
    ln2_shift,
    w_proj,
    proj_bias,
    segments,
    owners,
):
    dp_count = (lax.axis_size("y") * lax.axis_size("z"))
    ny, nz = lax.axis_size("y"), lax.axis_size("z")
    w_y = lax.all_gather(w_proj, "y", axis=0)
    w_proj_all = lax.all_gather(w_y, "z", axis=1).reshape(-1, w_proj.shape[1])
    gathered = lax.all_gather(tokens, TP, axis=0, tiled=True)
    tp_n = lax.axis_size("x") * lax.axis_size("core")
    nx, nc = lax.axis_size("x"), lax.axis_size("core")
    w_out_x = lax.all_to_all(jnp.broadcast_to(w_out[None], (nx,) + w_out.shape), "x", 0, 0, tiled=True)
    w_out_all = lax.all_to_all(jnp.broadcast_to(w_out_x[None], (nc,) + w_out_x.shape), "core", 0, 0, tiled=True)
    row_count = gathered.shape[0]
    normed = layer_norm(gathered, ln1_gain, ln1_shift).astype(jnp.bfloat16)
    heads_here = w_qkv.shape[1]
    heads_qkv = jnp.dot(
        normed, w_qkv.reshape(w_qkv.shape[0], -1), preferred_element_type=jnp.float32
    )
    heads_qkv = heads_qkv.astype(jnp.bfloat16).reshape(row_count, heads_here, -1)
    token_segs = jnp.repeat(segments[0], 4)
    context = attend(heads_qkv, token_segs).reshape(row_count, -1)
    tp_count = lax.axis_size("x") * lax.axis_size("core")
    local_rows = tokens.shape[0]
    context_mine = lax.all_to_all(context.reshape(tp_count, local_rows, -1), TP, 0, 0, tiled=True)
    out_heads = w_out_all.reshape(nc, nx, -1, w_out_all.shape[-1])
    context_xc = context_mine.reshape(nx, nc, local_rows, -1)
    attn = jnp.einsum("xcqd,cxdo->qo", context_xc, out_heads, preferred_element_type=jnp.float32)
    hidden = (tokens.astype(jnp.float32) + attn).astype(jnp.bfloat16)
    normed_two = layer_norm(hidden, ln2_gain, ln2_shift).astype(jnp.bfloat16)
    merged_mine = normed_two.reshape(local_rows // 4, -1)
    copies = jnp.broadcast_to(merged_mine[None], (tp_count,) + merged_mine.shape)
    merged = lax.all_to_all(copies, TP, 0, 0, tiled=True).reshape(-1, merged_mine.shape[1])
    groups = merged.shape[0]
    summed = jnp.dot(
        merged, w_proj_all, preferred_element_type=jnp.float32
    )
    projected = (summed + proj_bias).astype(jnp.bfloat16)
    dests = owners[:, 0]
    onehot = (dests[:, None] == jnp.arange(dp_count, dtype=jnp.int32)[None, :]).astype(jnp.int32)
    earlier = jnp.cumsum(onehot, axis=0) - onehot
    position = jnp.sum(earlier * onehot, axis=1)
    capacity = 2 * groups // dp_count
    slot_index = dests * capacity + position
    scatter_table = (
        slot_index[None, :] == jnp.arange(dp_count * capacity, dtype=jnp.int32)[:, None]
    ).astype(jnp.bfloat16)
    outgoing = jnp.dot(scatter_table, projected, preferred_element_type=jnp.float32).astype(
        jnp.bfloat16
    )
    outgoing = outgoing.reshape(dp_count, capacity, -1)
    arrived = lax.all_to_all(outgoing, DP, split_axis=0, concat_axis=0, tiled=True)
    return arrived.reshape(dp_count * capacity, -1)


def solution(mesh):
    return jax.shard_map(
        shards,
        mesh=Mesh(mesh.devices.reshape(4, 16, 4, 2), ("y", "z", "x", "core")),
        in_specs=(
            P(DP + TP, None),
            P(),
            P(),
            P(None, TP, None),
            P(TP, None, None),
            P(),
            P(),
            P(DP, TP),
            P(TP),
            P(DP, None),
            P(DP, None),
        ),
        out_specs=P(DP, TP),
        check_vma=False,
    )
```
